256 devices in a mesh: wall: 8 (over x, z_hi), span: 4 (over y), chord: 8 (over z_lo, core).
Axes of the slice: x: 4, y: 4, z: 8 (z_hi: 2, z_lo: 4; z = z_hi * 4 + z_lo), core: 2. Of those that a mesh axis runs over, the one named last changes fastest.
Arguments:
- source: float32 [4, 16, 32, 4, 320], P('span', 'chord', 'wall'), may hold values from -1.8 to 1.8
- adjoint_start: float32 [4, 16, 32, 4, 320], P('span', 'chord', 'wall'), may hold values from -6 to 6
- pivot_inverse: float32 [4, 16, 32, 320, 320], P('span', 'chord', 'wall'), as said below
- upper_block: float32 [4, 16, 32, 320, 320], P('span', 'chord', 'wall'), may hold values from -0.3125 to 0.3125
- lower_block: float32 [4, 16, 32, 320, 320], P('span', 'chord', 'wall'), may hold values from -0.3125 to 0.3125
- face_coupling: float32 [4, 80, 320], replicated, may hold values from -0.03125 to 0.03125
Outputs:
- adjoint: float32 [4, 16, 32, 4, 320], P('span', 'chord', 'wall')
The draws below stay inside these ranges and needn't reach their ends.
Inputs may be any that keep to these rules, and one draw needn't show every extreme that they name: `pivot_inverse`: each block equals 0.9 times the identity plus independent noise of root-mean-square 0.3 times 320 ** -0.5 an entry.
All inputs are finite; a program needn't handle non-finite values.
Results may differ from the reference program's by a relative error of at most 0.0003.
Values sent between devices are 32-bit elements; how exact they have to be, the bound alone decides.
No kernel may reach another device: no remote copies, remote signals or barrier semaphores. Data moves between devices by JAX's collectives and lax.ppermute only.
A program may use at most 128 MiB of HBM per device.

```python
import math
import jax
import jax.numpy as jnp
from jax import lax

NV = 5
P1 = 4
B = 320
FACE = 80
OBJ = 4
SWEEPS = 2
NE = 32
NSP = 4
NCH = 16


def draw_pivot_inverse(key, part):
    shape = (NSP, NCH, NE, B, B)
    eye_table = (lax.broadcasted_iota(jnp.int32, (B, B), 0) == lax.broadcasted_iota(jnp.int32, (B, B), 1)).astype(jnp.float32)
    noise = jax.random.normal(key, shape, jnp.float32) * (0.3 / math.sqrt(B))
    return 0.9 * eye_table + noise


def block_levels(stream_key, dims, cuts, low, high):
    gain = 1.0
    for axis_at, blocks in cuts:
        draws = jax.random.uniform(jax.random.fold_in(jax.random.fold_in(stream_key, 6), axis_at), (blocks,), jnp.float32, low / len(cuts), high / len(cuts))
        gain = gain * jnp.repeat(jnp.exp(draws), dims[axis_at] // blocks).reshape((-1,) + (1,) * (len(dims) - 1 - axis_at))
    return gain


def normal_values(key, dims, deviation, reach, cuts=(), held_as=jnp.bfloat16):
    entries = deviation * jax.random.normal(key, dims, jnp.float32)
    if cuts:
        entries = entries * block_levels(key, dims, cuts, -0.22, 0.18)
    return jnp.clip(entries, -reach, reach).astype(held_as)


def setup_inputs(seed: int = 0) -> dict:
    splits = jax.random.split(jax.random.key(seed), 7)
    return {
        "source": normal_values(splits[0], (NSP, NCH, NE, OBJ, B), 0.3, 1.8, ((0, 4), (1, 8), (2, 8)), jnp.float32),
        "adjoint_start": normal_values(splits[1], (NSP, NCH, NE, OBJ, B), 1.0, 6.0, ((0, 4), (1, 8), (2, 8)), jnp.float32),
        "pivot_inverse": draw_pivot_inverse(jax.random.fold_in(splits[6], 71), 0),
        "upper_block": normal_values(splits[3], (NSP, NCH, NE, B, B), B ** -0.5, 0.3125, ((0, 4), (1, 8), (2, 8)), jnp.float32),
        "lower_block": normal_values(splits[4], (NSP, NCH, NE, B, B), (B + B // 8) ** -0.5, 0.3125, ((0, 4), (1, 8), (2, 8)), jnp.float32),
        "face_coupling": normal_values(splits[5], (4, FACE, B), (400 * FACE) ** -0.5, 0.03125, (), jnp.float32),
    }


def face_traces(values):
    lead = values.shape[:4]
    shaped = values.reshape(lead + (NV, P1, P1, P1))
    flat = lead + (FACE,)
    return (shaped[..., :, 0, :, :].reshape(flat), shaped[..., :, P1 - 1, :, :].reshape(flat),
            shaped[..., :, :, 0, :].reshape(flat), shaped[..., :, :, P1 - 1, :].reshape(flat))


def from_next(values, axis):
    rest = lax.slice_in_dim(values, 1, values.shape[axis], axis=axis)
    blank = jnp.zeros_like(lax.slice_in_dim(values, 0, 1, axis=axis))
    return jnp.concatenate([rest, blank], axis=axis)


def from_prev(values, axis):
    rest = lax.slice_in_dim(values, 0, values.shape[axis] - 1, axis=axis)
    blank = jnp.zeros_like(lax.slice_in_dim(values, 0, 1, axis=axis))
    return jnp.concatenate([blank, rest], axis=axis)


def reference(source, adjoint_start, pivot_inverse, upper_block, lower_block, face_coupling):
    precise = lax.Precision.HIGHEST
    adjoint = adjoint_start
    pivots = jnp.moveaxis(pivot_inverse, 2, 0)
    uppers = jnp.moveaxis(upper_block, 2, 0)
    lowers = jnp.moveaxis(lower_block, 2, 0)
    for sweep_index in range(SWEEPS):
        low_span, high_span, low_chord, high_chord = face_traces(adjoint)
        neighbours = (from_next(low_span, 0), from_prev(high_span, 0),
                      from_next(low_chord, 1), from_prev(high_chord, 1))
        lateral = jnp.zeros_like(source)
        for which in range(4):
            lateral = lateral + jnp.einsum('scerf,fb->scerb', neighbours[which], face_coupling[which], precision=precise)
        right_side = jnp.moveaxis(source - lateral, 2, 0)

        def forward_step(carried, pieces):
            right_piece, pivot_piece, upper_piece = pieces
            value = jnp.einsum('scrb,scbk->scrk', right_piece - carried, pivot_piece, precision=precise)
            return jnp.einsum('scrb,scbk->scrk', value, upper_piece, precision=precise), value

        start = jnp.zeros(right_side.shape[1:], jnp.float32)
        unused, forward = lax.scan(forward_step, start, (right_side, pivots, uppers))

        def backward_step(carried, pieces):
            forward_piece, lower_piece = pieces
            value = forward_piece - carried
            return jnp.einsum('scrb,scbk->scrk', value, lower_piece, precision=precise), value

        unused, result = lax.scan(backward_step, start, (forward, lowers), reverse=True)
        adjoint = jnp.moveaxis(result, 0, 2)
    return adjoint
```

```python
import jax
import jax.numpy as jnp
from jax import lax
from jax.sharding import PartitionSpec as P

NV = 5
P1 = 4
FACE = 80
SWEEPS = 2
HI = lax.Precision.HIGHEST


def from_behind(block, axis, distance):
    devices = range(lax.axis_size(axis))
    route = [(i - distance, i) for i in devices if i - distance in devices]
    return lax.ppermute(block, axis, route)


def shift_in(values, axis, dim, step):
    count = values.shape[dim]
    if step > 0:
        edge = lax.slice_in_dim(values, 0, 1, axis=dim)
        incoming = from_behind(edge, axis, -1)
        rest = lax.slice_in_dim(values, 1, count, axis=dim)
        return jnp.concatenate([rest, incoming], axis=dim)
    edge = lax.slice_in_dim(values, count - 1, count, axis=dim)
    incoming = from_behind(edge, axis, 1)
    rest = lax.slice_in_dim(values, 0, count - 1, axis=dim)
    return jnp.concatenate([incoming, rest], axis=dim)


def faces(values):
    lead = values.shape[:4]
    shaped = values.reshape(lead + (NV, P1, P1, P1))
    flat = lead + (FACE,)
    return (
        shaped[..., :, 0, :, :].reshape(flat),
        shaped[..., :, P1 - 1, :, :].reshape(flat),
        shaped[..., :, :, 0, :].reshape(flat),
        shaped[..., :, :, P1 - 1, :].reshape(flat),
    )


def rows(vectors, matrix):
    return jnp.einsum("scrb,scbk->scrk", vectors, matrix, precision=HI)


def mats(left, right):
    return jnp.einsum("scij,scjk->scik", left, right, precision=HI)


def lateral_of(adjoint, coupling):
    low_span, high_span, low_chord, high_chord = faces(adjoint)
    stacked = jnp.concatenate(
        [
            shift_in(low_span, "span", 0, 1),
            shift_in(high_span, "span", 0, -1),
            shift_in(low_chord, "chord", 1, 1),
            shift_in(high_chord, "chord", 1, -1),
        ],
        axis=-1,
    )
    return jnp.einsum("scerf,fb->scerb", stacked, coupling, precision=HI)


def carry_plan(local_mat, step, reach):
    got = [from_behind(local_mat, "wall", step * j) for j in range(1, reach + 1)]
    chain = []
    prod = None
    for j in range(2, reach + 1):
        prod = got[0] if prod is None else mats(got[j - 2], prod)
        chain.append(prod)
    jump = got[reach - 1] if prod is None else mats(got[reach - 1], prod)
    return chain, jump


def carry_in(offset, chain, jump, step, reach, count):
    got = [from_behind(offset, "wall", step * j) for j in range(1, reach + 1)]
    first = got[0]
    for j in range(2, reach + 1):
        first = first + rows(got[j - 1], chain[j - 2])
    if count - 1 <= reach:
        return first
    far = from_behind(first, "wall", step * reach)
    return first + rows(far, jump)


def local(source, adjoint_start, pivot_inverse, upper_block, lower_block, face_coupling):
    lines_span, lines_chord, elements, objectives, width = source.shape
    count = lax.axis_size("wall")
    reach = max(1, (count - 1 + 1) // 2)
    coupling = face_coupling.reshape(4 * FACE, width)

    heads = []
    acc = pivot_inverse[:, :, 0]
    for element in range(elements):
        heads.append(acc)
        prod = mats(acc, upper_block[:, :, element])
        if element + 1 < elements:
            acc = -mats(prod, pivot_inverse[:, :, element + 1])
    forward_mat = -prod
    head_cat = jnp.stack(heads, axis=2)

    tails = [None] * elements
    acc = None
    for element in reversed(range(elements)):
        tails[element] = acc
        if acc is None:
            acc = -lower_block[:, :, element]
        else:
            acc = -mats(acc, lower_block[:, :, element])
    backward_mat = acc
    tail_cat = jnp.stack(tails[: elements - 1], axis=2) if elements > 1 else None

    fchain, fjump = carry_plan(forward_mat, 1, reach)
    bchain, bjump = carry_plan(backward_mat, -1, reach)

    adjoint = adjoint_start
    for sweep_index in range(SWEEPS):
        right_side = source - lateral_of(adjoint, coupling)

        values = []
        carried = None
        for element in range(elements):
            piece = right_side[:, :, element]
            if carried is not None:
                piece = piece - carried
            value = rows(piece, pivot_inverse[:, :, element])
            carried = rows(value, upper_block[:, :, element])
            values.append(value)
        base = jnp.stack(values, axis=2)
        c_in = carry_in(carried, fchain, fjump, 1, reach, count)
        forward = base - jnp.einsum("scrb,scebk->scerk", c_in, head_cat, precision=HI)

        values = [None] * elements
        carried = None
        for element in reversed(range(elements)):
            value = forward[:, :, element]
            if carried is not None:
                value = value - carried
            carried = rows(value, lower_block[:, :, element])
            values[element] = value
        k_in = carry_in(carried, bchain, bjump, -1, reach, count)
        if tail_cat is not None:
            fix = jnp.einsum("scrb,scebk->scerk", k_in, tail_cat, precision=HI)
            fix = jnp.concatenate([fix, k_in[:, :, None]], axis=2)
        else:
            fix = k_in[:, :, None]
        adjoint = jnp.stack(values, axis=2) - fix
    return adjoint


def solution(mesh):
    return jax.shard_map(
        local,
        mesh=mesh,
        in_specs=(
            P("span", "chord", "wall", None, None),
            P("span", "chord", "wall", None, None),
            P("span", "chord", "wall", None, None),
            P("span", "chord", "wall", None, None),
            P("span", "chord", "wall", None, None),
            P(),
        ),
        out_specs=P("span", "chord", "wall", None, None),
        check_vma=False,
    )
```

```python
import jax
import jax.numpy as jnp
from jax import lax
from jax.sharding import PartitionSpec as P

NV = 5
P1 = 4
FACE = 80
SWEEPS = 2
HI = lax.Precision.HIGHEST


def from_behind(block, axis, distance):
    devices = range(lax.axis_size(axis))
    route = [(i - distance, i) for i in devices if i - distance in devices]
    return lax.ppermute(block, axis, route)


def shift_in(values, axis, dim, step):
    count = values.shape[dim]
    if step > 0:
        edge = lax.slice_in_dim(values, 0, 1, axis=dim)
        incoming = from_behind(edge, axis, -1)
        rest = lax.slice_in_dim(values, 1, count, axis=dim)
        return jnp.concatenate([rest, incoming], axis=dim)
    edge = lax.slice_in_dim(values, count - 1, count, axis=dim)
    incoming = from_behind(edge, axis, 1)
    rest = lax.slice_in_dim(values, 0, count - 1, axis=dim)
    return jnp.concatenate([incoming, rest], axis=dim)


def faces(values):
    lead = values.shape[:4]
    shaped = values.reshape(lead + (NV, P1, P1, P1))
    flat = lead + (FACE,)
    return (
        shaped[..., :, 0, :, :].reshape(flat),
        shaped[..., :, P1 - 1, :, :].reshape(flat),
        shaped[..., :, :, 0, :].reshape(flat),
        shaped[..., :, :, P1 - 1, :].reshape(flat),
    )


def rows(vectors, matrix):
    return jnp.einsum("scrb,scbk->scrk", vectors, matrix, precision=HI)


def mats(left, right):
    return jnp.einsum("scij,scjk->scik", left, right, precision=HI)


def lateral_of(adjoint, coupling):
    low_span, high_span, low_chord, high_chord = faces(adjoint)
    stacked = jnp.concatenate(
        [
            shift_in(low_span, "span", 0, 1),
            shift_in(high_span, "span", 0, -1),
            shift_in(low_chord, "chord", 1, 1),
            shift_in(high_chord, "chord", 1, -1),
        ],
        axis=-1,
    )
    return jnp.einsum("scerf,fb->scerb", stacked, coupling, precision=HI)


def carry_plan(local_mat, step, count):
    prev = from_behind(local_mat, "wall", step)
    pair = mats(prev, local_mat)
    terms = [prev]
    for j in range(1, (count - 1) // 2):
        far = from_behind(pair, "wall", 2 * j * step)
        terms.append(mats(far, terms[-1]))
    return jnp.concatenate(terms, axis=2) if len(terms) > 1 else terms[0]


def carry_in(offset, local_mat, terms, step, count):
    near = from_behind(offset, "wall", step)
    reach = (count - 1) // 2
    if reach == 0:
        return near
    paired = offset + rows(near, local_mat)
    got = [from_behind(paired, "wall", 2 * j * step) for j in range(1, reach + 1)]
    return near + rows(jnp.concatenate(got, axis=-1), terms)


def local(source, adjoint_start, pivot_inverse, upper_block, lower_block, face_coupling):
    lines_span, lines_chord, elements, objectives, width = source.shape
    count = lax.axis_size("wall")
    coupling = face_coupling.reshape(4 * FACE, width)

    heads = []
    acc = pivot_inverse[:, :, 0]
    for element in range(elements):
        heads.append(acc)
        prod = mats(acc, upper_block[:, :, element])
        if element + 1 < elements:
            acc = -mats(prod, pivot_inverse[:, :, element + 1])
    forward_mat = -prod
    head_cat = jnp.stack(heads, axis=2)

    tails = [None] * elements
    acc = None
    for element in reversed(range(elements)):
        tails[element] = acc
        if acc is None:
            acc = -lower_block[:, :, element]
        else:
            acc = -mats(acc, lower_block[:, :, element])
    backward_mat = acc
    tail_cat = jnp.stack(tails[: elements - 1], axis=2) if elements > 1 else None

    fterms = carry_plan(forward_mat, 1, count)
    bterms = carry_plan(backward_mat, -1, count)

    adjoint = adjoint_start
    for sweep_index in range(SWEEPS):
        right_side = source - lateral_of(adjoint, coupling)

        values = []
        carried = None
        for element in range(elements):
            piece = right_side[:, :, element]
            if carried is not None:
                piece = piece - carried
            value = rows(piece, pivot_inverse[:, :, element])
            carried = rows(value, upper_block[:, :, element])
            values.append(value)
        base = jnp.stack(values, axis=2)
        c_in = carry_in(carried, forward_mat, fterms, 1, count)
        forward = base - jnp.einsum("scrb,scebk->scerk", c_in, head_cat, precision=HI)

        values = [None] * elements
        carried = None
        for element in reversed(range(elements)):
            value = forward[:, :, element]
            if carried is not None:
                value = value - carried
            carried = rows(value, lower_block[:, :, element])
            values[element] = value
        k_in = carry_in(carried, backward_mat, bterms, -1, count)
        if tail_cat is not None:
            fix = jnp.einsum("scrb,scebk->scerk", k_in, tail_cat, precision=HI)
            fix = jnp.concatenate([fix, k_in[:, :, None]], axis=2)
        else:
            fix = k_in[:, :, None]
        adjoint = jnp.stack(values, axis=2) - fix
    return adjoint


def solution(mesh):
    return jax.shard_map(
        local,
        mesh=mesh,
        in_specs=(
            P("span", "chord", "wall", None, None),
            P("span", "chord", "wall", None, None),
            P("span", "chord", "wall", None, None),
            P("span", "chord", "wall", None, None),
            P("span", "chord", "wall", None, None),
            P(),
        ),
        out_specs=P("span", "chord", "wall", None, None),
        check_vma=False,
    )
```

```python
import jax
import jax.numpy as jnp
from jax import lax
from jax.sharding import PartitionSpec as P

NV = 5
P1 = 4
FACE = 80
SWEEPS = 2
HI = lax.Precision.HIGHEST


def from_behind(block, axis, distance):
    devices = range(lax.axis_size(axis))
    route = [(i - distance, i) for i in devices if i - distance in devices]
    return lax.ppermute(block, axis, route)


def shift_in(values, axis, dim, step):
    count = values.shape[dim]
    if step > 0:
        edge = lax.slice_in_dim(values, 0, 1, axis=dim)
        incoming = from_behind(edge, axis, -1)
        rest = lax.slice_in_dim(values, 1, count, axis=dim)
        return jnp.concatenate([rest, incoming], axis=dim)
    edge = lax.slice_in_dim(values, count - 1, count, axis=dim)
    incoming = from_behind(edge, axis, 1)
    rest = lax.slice_in_dim(values, 0, count - 1, axis=dim)
    return jnp.concatenate([incoming, rest], axis=dim)


def faces(values):
    lead = values.shape[:4]
    shaped = values.reshape(lead + (NV, P1, P1, P1))
    flat = lead + (FACE,)
    return (
        shaped[..., :, 0, :, :].reshape(flat),
        shaped[..., :, P1 - 1, :, :].reshape(flat),
        shaped[..., :, :, 0, :].reshape(flat),
        shaped[..., :, :, P1 - 1, :].reshape(flat),
    )


def rows(vectors, matrix):
    return jnp.einsum("scrb,scbk->scrk", vectors, matrix, precision=HI)


def mats(left, right):
    return jnp.einsum("scij,scjk->scik", left, right, precision=HI)


def coupling_blocks(face_coupling, width):
    fc = face_coupling.reshape(4, NV, P1 * P1, width)
    span_face = lambda m: m.reshape(NV, 1, P1, P1, width)
    chord_face = lambda m: m.reshape(NV, P1, 1, P1, width)
    blocks = [
        jnp.pad(span_face(fc[0]), ((0, 0), (0, P1 - 1), (0, 0), (0, 0), (0, 0))),
        jnp.pad(span_face(fc[1]), ((0, 0), (P1 - 1, 0), (0, 0), (0, 0), (0, 0))),
        jnp.pad(chord_face(fc[2]), ((0, 0), (0, 0), (0, P1 - 1), (0, 0), (0, 0))),
        jnp.pad(chord_face(fc[3]), ((0, 0), (0, 0), (P1 - 1, 0), (0, 0), (0, 0))),
    ]
    return jnp.stack([b.reshape(width, width) for b in blocks], axis=1)


def lateral_of(adjoint, blocks):
    parts = jnp.einsum("scerb,bdk->dscerk", adjoint, blocks, precision=HI)
    return (
        shift_in(parts[0], "span", 0, 1)
        + shift_in(parts[1], "span", 0, -1)
        + shift_in(parts[2], "chord", 1, 1)
        + shift_in(parts[3], "chord", 1, -1)
    )


def prefix_products(stack):
    count = stack.shape[2]
    gap = 1
    while gap < count:
        head = lax.slice_in_dim(stack, 0, gap, axis=2)
        lhs = lax.slice_in_dim(stack, 0, count - gap, axis=2)
        rhs = lax.slice_in_dim(stack, gap, count, axis=2)
        joined = jnp.einsum("sceij,scejk->sceik", lhs, rhs, precision=HI)
        stack = jnp.concatenate([head, joined], axis=2)
        gap *= 2
    return stack


def carry_plan(local_mat, step, count):
    prev = from_behind(local_mat, "wall", step)
    pair = mats(prev, local_mat)
    terms = [prev]
    for j in range(1, (count - 1) // 2):
        far = from_behind(pair, "wall", 2 * j * step)
        terms.append(mats(far, terms[-1]))
    return jnp.concatenate(terms, axis=2) if len(terms) > 1 else terms[0]


def carry_in(offset, local_mat, terms, step, count):
    near = from_behind(offset, "wall", step)
    reach = (count - 1) // 2
    if reach == 0:
        return near
    paired = offset + rows(near, local_mat)
    got = [from_behind(paired, "wall", 2 * j * step) for j in range(1, reach + 1)]
    return near + rows(jnp.concatenate(got, axis=-1), terms)


def local(source, adjoint_start, pivot_inverse, upper_block, lower_block, face_coupling):
    lines_span, lines_chord, elements, objectives, width = source.shape
    count = lax.axis_size("wall")
    blocks = coupling_blocks(face_coupling, width)

    steps = jnp.einsum("scebk,scekj->scebj", pivot_inverse, upper_block, precision=HI)
    runs = prefix_products(steps)
    signs = jnp.array([(-1.0) ** e for e in range(elements)], jnp.float32)[:, None, None]
    if elements > 1:
        later = jnp.einsum("sceij,scejk->sceik", runs[:, :, : elements - 1],
                           pivot_inverse[:, :, 1:], precision=HI)
        head_cat = jnp.concatenate([pivot_inverse[:, :, :1], later], axis=2) * signs
    else:
        head_cat = pivot_inverse
    forward_mat = runs[:, :, elements - 1] * ((-1.0) ** elements)

    tails_run = prefix_products(lower_block[:, :, ::-1])
    backward_mat = tails_run[:, :, elements - 1] * ((-1.0) ** elements)
    if elements > 1:
        tail_cat = tails_run[:, :, elements - 2 :: -1] * signs[::-1][1:] * -1.0
    else:
        tail_cat = None

    fterms = carry_plan(forward_mat, 1, count)
    bterms = carry_plan(backward_mat, -1, count)

    adjoint = adjoint_start
    for sweep_index in range(SWEEPS):
        right_side = source - lateral_of(adjoint, blocks)

        values = []
        carried = None
        for element in range(elements):
            piece = right_side[:, :, element]
            if carried is not None:
                piece = piece - carried
            value = rows(piece, pivot_inverse[:, :, element])
            carried = rows(value, upper_block[:, :, element])
            values.append(value)
        base = jnp.stack(values, axis=2)
        c_in = carry_in(carried, forward_mat, fterms, 1, count)
        forward = base - jnp.einsum("scrb,scebk->scerk", c_in, head_cat, precision=HI)

        values = [None] * elements
        carried = None
        for element in reversed(range(elements)):
            value = forward[:, :, element]
            if carried is not None:
                value = value - carried
            carried = rows(value, lower_block[:, :, element])
            values[element] = value
        k_in = carry_in(carried, backward_mat, bterms, -1, count)
        if tail_cat is not None:
            fix = jnp.einsum("scrb,scebk->scerk", k_in, tail_cat, precision=HI)
            fix = jnp.concatenate([fix, k_in[:, :, None]], axis=2)
        else:
            fix = k_in[:, :, None]
        adjoint = jnp.stack(values, axis=2) - fix
    return adjoint


def solution(mesh):
    return jax.shard_map(
        local,
        mesh=mesh,
        in_specs=(
            P("span", "chord", "wall", None, None),
            P("span", "chord", "wall", None, None),
            P("span", "chord", "wall", None, None),
            P("span", "chord", "wall", None, None),
            P("span", "chord", "wall", None, None),
            P(),
        ),
        out_specs=P("span", "chord", "wall", None, None),
        check_vma=False,
    )
```

```python
import jax
import jax.numpy as jnp
from jax import lax
from jax.sharding import PartitionSpec as P

NV = 5
P1 = 4
FACE = 80
SWEEPS = 2
HI = lax.Precision.HIGHEST


def from_behind(block, axis, distance):
    devices = range(lax.axis_size(axis))
    route = [(i - distance, i) for i in devices if i - distance in devices]
    return lax.ppermute(block, axis, route)


def shift_in(values, axis, dim, step):
    count = values.shape[dim]
    if step > 0:
        edge = lax.slice_in_dim(values, 0, 1, axis=dim)
        incoming = from_behind(edge, axis, -1)
        rest = lax.slice_in_dim(values, 1, count, axis=dim)
        return jnp.concatenate([rest, incoming], axis=dim)
    edge = lax.slice_in_dim(values, count - 1, count, axis=dim)
    incoming = from_behind(edge, axis, 1)
    rest = lax.slice_in_dim(values, 0, count - 1, axis=dim)
    return jnp.concatenate([incoming, rest], axis=dim)


def faces(values):
    lead = values.shape[:4]
    shaped = values.reshape(lead + (NV, P1, P1, P1))
    flat = lead + (FACE,)
    return (
        shaped[..., :, 0, :, :].reshape(flat),
        shaped[..., :, P1 - 1, :, :].reshape(flat),
        shaped[..., :, :, 0, :].reshape(flat),
        shaped[..., :, :, P1 - 1, :].reshape(flat),
    )


def rows(vectors, matrix):
    return jnp.einsum("scrb,scbk->scrk", vectors, matrix, precision=HI)


def mats(left, right):
    return jnp.einsum("scij,scjk->scik", left, right, precision=HI)


def coupling_blocks(face_coupling, width):
    fc = face_coupling.reshape(4, NV, P1 * P1, width)
    span_face = lambda m: m.reshape(NV, 1, P1, P1, width)
    chord_face = lambda m: m.reshape(NV, P1, 1, P1, width)
    blocks = [
        jnp.pad(span_face(fc[0]), ((0, 0), (0, P1 - 1), (0, 0), (0, 0), (0, 0))),
        jnp.pad(span_face(fc[1]), ((0, 0), (P1 - 1, 0), (0, 0), (0, 0), (0, 0))),
        jnp.pad(chord_face(fc[2]), ((0, 0), (0, 0), (0, P1 - 1), (0, 0), (0, 0))),
        jnp.pad(chord_face(fc[3]), ((0, 0), (0, 0), (P1 - 1, 0), (0, 0), (0, 0))),
    ]
    return jnp.stack([b.reshape(width, width) for b in blocks], axis=1)


def lateral_of(adjoint, blocks):
    parts = jnp.einsum("scerb,bdk->dscerk", adjoint, blocks, precision=HI)
    return (
        shift_in(parts[0], "span", 0, 1)
        + shift_in(parts[1], "span", 0, -1)
        + shift_in(parts[2], "chord", 1, 1)
        + shift_in(parts[3], "chord", 1, -1)
    )


def carry_plan(local_mat, step):
    prev = from_behind(local_mat, "wall", step)
    return prev, mats(prev, local_mat)


def carry_in(offset, local_mat, prev, pair, step, count):
    near = from_behind(offset, "wall", step)
    hops = (count - 1) // 2
    if hops == 0:
        return near
    paired = offset + rows(near, local_mat)
    state = paired
    for hop in range(hops):
        got = from_behind(state, "wall", 2 * step)
        if hop + 1 < hops:
            state = paired + rows(got, pair)
    return near + rows(got, prev)


def local(source, adjoint_start, pivot_inverse, upper_block, lower_block, face_coupling):
    lines_span, lines_chord, elements, objectives, width = source.shape
    count = lax.axis_size("wall")
    blocks = coupling_blocks(face_coupling, width)

    heads = []
    acc = pivot_inverse[:, :, 0]
    for element in range(elements):
        heads.append(acc)
        prod = mats(acc, upper_block[:, :, element])
        if element + 1 < elements:
            acc = -mats(prod, pivot_inverse[:, :, element + 1])
    forward_mat = -prod
    head_cat = jnp.stack(heads, axis=2)
    fprev, fpair = carry_plan(forward_mat, 1)

    tails = [None] * elements
    acc = None
    for element in reversed(range(elements)):
        tails[element] = acc
        if acc is None:
            acc = -lower_block[:, :, element]
        else:
            acc = -mats(acc, lower_block[:, :, element])
    backward_mat = acc
    tail_cat = jnp.stack(tails[: elements - 1], axis=2) if elements > 1 else None
    bprev, bpair = carry_plan(backward_mat, -1)

    adjoint = adjoint_start
    for sweep_index in range(SWEEPS):
        right_side = source - lateral_of(adjoint, blocks)

        values = []
        carried = None
        for element in range(elements):
            piece = right_side[:, :, element]
            if carried is not None:
                piece = piece - carried
            value = rows(piece, pivot_inverse[:, :, element])
            carried = rows(value, upper_block[:, :, element])
            values.append(value)
        base = jnp.stack(values, axis=2)
        c_in = carry_in(carried, forward_mat, fprev, fpair, 1, count)
        forward = base - jnp.einsum("scrb,scebk->scerk", c_in, head_cat, precision=HI)

        values = [None] * elements
        carried = None
        for element in reversed(range(elements)):
            value = forward[:, :, element]
            if carried is not None:
                value = value - carried
            carried = rows(value, lower_block[:, :, element])
            values[element] = value
        k_in = carry_in(carried, backward_mat, bprev, bpair, -1, count)
        if tail_cat is not None:
            fix = jnp.einsum("scrb,scebk->scerk", k_in, tail_cat, precision=HI)
            fix = jnp.concatenate([fix, k_in[:, :, None]], axis=2)
        else:
            fix = k_in[:, :, None]
        adjoint = jnp.stack(values, axis=2) - fix
    return adjoint


def solution(mesh):
    return jax.shard_map(
        local,
        mesh=mesh,
        in_specs=(
            P("span", "chord", "wall", None, None),
            P("span", "chord", "wall", None, None),
            P("span", "chord", "wall", None, None),
            P("span", "chord", "wall", None, None),
            P("span", "chord", "wall", None, None),
            P(),
        ),
        out_specs=P("span", "chord", "wall", None, None),
        check_vma=False,
    )
```

```python
import jax
import jax.numpy as jnp
from jax import lax
from jax.sharding import PartitionSpec as P

NV = 5
P1 = 4
FACE = 80
SWEEPS = 2
HI = lax.Precision.HIGHEST


def from_behind(block, axis, distance):
    devices = range(lax.axis_size(axis))
    route = [(i - distance, i) for i in devices if i - distance in devices]
    return lax.ppermute(block, axis, route)


def shift_in(values, axis, dim, step):
    count = values.shape[dim]
    if step > 0:
        edge = lax.slice_in_dim(values, 0, 1, axis=dim)
        incoming = from_behind(edge, axis, -1)
        rest = lax.slice_in_dim(values, 1, count, axis=dim)
        return jnp.concatenate([rest, incoming], axis=dim)
    edge = lax.slice_in_dim(values, count - 1, count, axis=dim)
    incoming = from_behind(edge, axis, 1)
    rest = lax.slice_in_dim(values, 0, count - 1, axis=dim)
    return jnp.concatenate([incoming, rest], axis=dim)


def faces(values):
    lead = values.shape[:4]
    shaped = values.reshape(lead + (NV, P1, P1, P1))
    flat = lead + (FACE,)
    return (
        shaped[..., :, 0, :, :].reshape(flat),
        shaped[..., :, P1 - 1, :, :].reshape(flat),
        shaped[..., :, :, 0, :].reshape(flat),
        shaped[..., :, :, P1 - 1, :].reshape(flat),
    )


def rows(vectors, matrix):
    return jnp.einsum("scrb,scbk->scrk", vectors, matrix, precision=HI)


def mats(left, right):
    return jnp.einsum("scij,scjk->scik", left, right, precision=HI)


def coupling_blocks(face_coupling, width):
    fc = face_coupling.reshape(4, NV, P1 * P1, width)
    span_face = lambda m: m.reshape(NV, 1, P1, P1, width)
    chord_face = lambda m: m.reshape(NV, P1, 1, P1, width)
    blocks = [
        jnp.pad(span_face(fc[0]), ((0, 0), (0, P1 - 1), (0, 0), (0, 0), (0, 0))),
        jnp.pad(span_face(fc[1]), ((0, 0), (P1 - 1, 0), (0, 0), (0, 0), (0, 0))),
        jnp.pad(chord_face(fc[2]), ((0, 0), (0, 0), (0, P1 - 1), (0, 0), (0, 0))),
        jnp.pad(chord_face(fc[3]), ((0, 0), (0, 0), (P1 - 1, 0), (0, 0), (0, 0))),
    ]
    return jnp.stack([b.reshape(width, width) for b in blocks], axis=1)


def lateral_of(adjoint, blocks):
    parts = jnp.einsum("scerb,bdk->dscerk", adjoint, blocks, precision=HI)
    return (
        shift_in(parts[0], "span", 0, 1)
        + shift_in(parts[1], "span", 0, -1)
        + shift_in(parts[2], "chord", 1, 1)
        + shift_in(parts[3], "chord", 1, -1)
    )


def carry_plan(local_mat, step):
    prev = from_behind(local_mat, "wall", step)
    return prev, mats(prev, local_mat)


def carry_in(offset, local_mat, prev, pair, step, count):
    near = from_behind(offset, "wall", step)
    hops = (count - 1) // 2
    if hops == 0:
        return near
    paired = offset + rows(near, local_mat)
    state = paired
    for hop in range(hops):
        got = from_behind(state, "wall", 2 * step)
        if hop + 1 < hops:
            state = paired + rows(got, pair)
    return near + rows(got, prev)


def local(source, adjoint_start, pivot_inverse, upper_block, lower_block, face_coupling):
    lines_span, lines_chord, elements, objectives, width = source.shape
    count = lax.axis_size("wall")
    blocks = coupling_blocks(face_coupling, width)

    heads = []
    acc = pivot_inverse[:, :, 0]
    for element in range(elements):
        heads.append(acc)
        prod = mats(acc, upper_block[:, :, element])
        if element + 1 < elements:
            acc = -mats(prod, pivot_inverse[:, :, element + 1])
    forward_mat = -prod
    head_cat = jnp.stack(heads, axis=2)
    fprev, fpair = carry_plan(forward_mat, 1)

    tails = [None] * elements
    acc = None
    for element in reversed(range(elements)):
        tails[element] = acc
        if acc is None:
            acc = -lower_block[:, :, element]
        else:
            acc = -mats(acc, lower_block[:, :, element])
    backward_mat = acc
    tail_cat = jnp.stack(tails[: elements - 1], axis=2) if elements > 1 else None
    backward_mat, _ = lax.optimization_barrier((backward_mat, fprev))
    bprev, bpair = carry_plan(backward_mat, -1)

    adjoint = adjoint_start
    for sweep_index in range(SWEEPS):
        right_side = source - lateral_of(adjoint, blocks)

        values = []
        carried = None
        for element in range(elements):
            piece = right_side[:, :, element]
            if carried is not None:
                piece = piece - carried
            value = rows(piece, pivot_inverse[:, :, element])
            carried = rows(value, upper_block[:, :, element])
            values.append(value)
        base = jnp.stack(values, axis=2)
        c_in = carry_in(carried, forward_mat, fprev, fpair, 1, count)
        forward = base - jnp.einsum("scrb,scebk->scerk", c_in, head_cat, precision=HI)

        values = [None] * elements
        carried = None
        for element in reversed(range(elements)):
            value = forward[:, :, element]
            if carried is not None:
                value = value - carried
            carried = rows(value, lower_block[:, :, element])
            values[element] = value
        k_in = carry_in(carried, backward_mat, bprev, bpair, -1, count)
        if tail_cat is not None:
            fix = jnp.einsum("scrb,scebk->scerk", k_in, tail_cat, precision=HI)
            fix = jnp.concatenate([fix, k_in[:, :, None]], axis=2)
        else:
            fix = k_in[:, :, None]
        adjoint = jnp.stack(values, axis=2) - fix
    return adjoint


def solution(mesh):
    return jax.shard_map(
        local,
        mesh=mesh,
        in_specs=(
            P("span", "chord", "wall", None, None),
            P("span", "chord", "wall", None, None),
            P("span", "chord", "wall", None, None),
            P("span", "chord", "wall", None, None),
            P("span", "chord", "wall", None, None),
            P(),
        ),
        out_specs=P("span", "chord", "wall", None, None),
        check_vma=False,
    )
```

```python
import jax
import jax.numpy as jnp
from jax import lax
from jax.sharding import PartitionSpec as P

NV = 5
P1 = 4
FACE = 80
SWEEPS = 2
HI = lax.Precision.HIGHEST


def from_behind(block, axis, distance):
    devices = range(lax.axis_size(axis))
    route = [(i - distance, i) for i in devices if i - distance in devices]
    return lax.ppermute(block, axis, route)


def shift_in(values, axis, dim, step):
    count = values.shape[dim]
    if step > 0:
        edge = lax.slice_in_dim(values, 0, 1, axis=dim)
        incoming = from_behind(edge, axis, -1)
        rest = lax.slice_in_dim(values, 1, count, axis=dim)
        return jnp.concatenate([rest, incoming], axis=dim)
    edge = lax.slice_in_dim(values, count - 1, count, axis=dim)
    incoming = from_behind(edge, axis, 1)
    rest = lax.slice_in_dim(values, 0, count - 1, axis=dim)
    return jnp.concatenate([incoming, rest], axis=dim)


def faces(values):
    lead = values.shape[:4]
    shaped = values.reshape(lead + (NV, P1, P1, P1))
    flat = lead + (FACE,)
    return (
        shaped[..., :, 0, :, :].reshape(flat),
        shaped[..., :, P1 - 1, :, :].reshape(flat),
        shaped[..., :, :, 0, :].reshape(flat),
        shaped[..., :, :, P1 - 1, :].reshape(flat),
    )


def rows(vectors, matrix):
    return jnp.einsum("scrb,scbk->scrk", vectors, matrix, precision=HI)


def mats(left, right):
    return jnp.einsum("scij,scjk->scik", left, right, precision=HI)


def coupling_blocks(face_coupling, width):
    fc = face_coupling.reshape(4, NV, P1 * P1, width)
    span_face = lambda m: m.reshape(NV, 1, P1, P1, width)
    chord_face = lambda m: m.reshape(NV, P1, 1, P1, width)
    blocks = [
        jnp.pad(span_face(fc[0]), ((0, 0), (0, P1 - 1), (0, 0), (0, 0), (0, 0))),
        jnp.pad(span_face(fc[1]), ((0, 0), (P1 - 1, 0), (0, 0), (0, 0), (0, 0))),
        jnp.pad(chord_face(fc[2]), ((0, 0), (0, 0), (0, P1 - 1), (0, 0), (0, 0))),
        jnp.pad(chord_face(fc[3]), ((0, 0), (0, 0), (P1 - 1, 0), (0, 0), (0, 0))),
    ]
    return jnp.stack([b.reshape(width, width) for b in blocks], axis=1)


def lateral_of(adjoint, blocks):
    parts = jnp.einsum("scerb,bdk->dscerk", adjoint, blocks, precision=HI)
    return (
        shift_in(parts[0], "span", 0, 1)
        + shift_in(parts[1], "span", 0, -1)
        + shift_in(parts[2], "chord", 1, 1)
        + shift_in(parts[3], "chord", 1, -1)
    )


def carry_plan(local_mat, step, count):
    prev = from_behind(local_mat, "wall", step)
    pair = mats(prev, local_mat)
    if 5 <= count <= 8:
        return prev, pair, mats(from_behind(pair, "wall", 2 * step), prev)
    return prev, pair, None


def carry_in(offset, local_mat, plan, step, count):
    prev, pair, jump = plan
    near = from_behind(offset, "wall", step)
    hops = (count - 1) // 2
    if hops == 0:
        return near
    paired = offset + rows(near, local_mat)
    if jump is not None:
        got = from_behind(paired, "wall", 2 * step)
        both = paired + rows(got, pair)
        far = from_behind(both, "wall", 4 * step)
        return near + rows(jnp.concatenate([got, far], axis=-1), jnp.concatenate([prev, jump], axis=2))
    state = paired
    for hop in range(hops):
        got = from_behind(state, "wall", 2 * step)
        if hop + 1 < hops:
            state = paired + rows(got, pair)
    return near + rows(got, prev)


def local(source, adjoint_start, pivot_inverse, upper_block, lower_block, face_coupling):
    lines_span, lines_chord, elements, objectives, width = source.shape
    count = lax.axis_size("wall")
    blocks = coupling_blocks(face_coupling, width)

    heads = []
    acc = pivot_inverse[:, :, 0]
    for element in range(elements):
        heads.append(acc)
        prod = mats(acc, upper_block[:, :, element])
        if element + 1 < elements:
            acc = -mats(prod, pivot_inverse[:, :, element + 1])
    forward_mat = -prod
    head_cat = jnp.stack(heads, axis=2)
    fplan = carry_plan(forward_mat, 1, count)

    tails = [None] * elements
    acc = None
    for element in reversed(range(elements)):
        tails[element] = acc
        if acc is None:
            acc = -lower_block[:, :, element]
        else:
            acc = -mats(acc, lower_block[:, :, element])
    backward_mat = acc
    tail_cat = jnp.stack(tails[: elements - 1], axis=2) if elements > 1 else None
    bplan = carry_plan(backward_mat, -1, count)

    adjoint = adjoint_start
    for sweep_index in range(SWEEPS):
        right_side = source - lateral_of(adjoint, blocks)

        values = []
        carried = None
        for element in range(elements):
            piece = right_side[:, :, element]
            if carried is not None:
                piece = piece - carried
            value = rows(piece, pivot_inverse[:, :, element])
            carried = rows(value, upper_block[:, :, element])
            values.append(value)
        base = jnp.stack(values, axis=2)
        c_in = carry_in(carried, forward_mat, fplan, 1, count)
        forward = base - jnp.einsum("scrb,scebk->scerk", c_in, head_cat, precision=HI)

        values = [None] * elements
        carried = None
        for element in reversed(range(elements)):
            value = forward[:, :, element]
            if carried is not None:
                value = value - carried
            carried = rows(value, lower_block[:, :, element])
            values[element] = value
        k_in = carry_in(carried, backward_mat, bplan, -1, count)
        if tail_cat is not None:
            fix = jnp.einsum("scrb,scebk->scerk", k_in, tail_cat, precision=HI)
            fix = jnp.concatenate([fix, k_in[:, :, None]], axis=2)
        else:
            fix = k_in[:, :, None]
        adjoint = jnp.stack(values, axis=2) - fix
    return adjoint


def solution(mesh):
    return jax.shard_map(
        local,
        mesh=mesh,
        in_specs=(
            P("span", "chord", "wall", None, None),
            P("span", "chord", "wall", None, None),
            P("span", "chord", "wall", None, None),
            P("span", "chord", "wall", None, None),
            P("span", "chord", "wall", None, None),
            P(),
        ),
        out_specs=P("span", "chord", "wall", None, None),
        check_vma=False,
    )
```
